128 devices in a mesh: row: 8 (over x, core), col: 16 (over z, y).
Axes of the slice: x: 4, y: 4, z: 4, core: 2. Of those that a mesh axis runs over, the one named last changes fastest.
Arguments:
- rhs: float32 [24, 32768], P(None, 'col'), may hold values from -6 to 6
- noise_var: float32 [32768], P('col'), may hold values from 0.9 to 3.6
- block_rows: int32 [8, 2], P('row'), may hold values from 0 to 15, as said below
- kernel_blocks: bfloat16 [8, 16, 2, 1, 2048, 2048], P('row', 'col'), may hold values from -0.0078125 to 0.0078125
Outputs:
- solution_field: float32 [24, 32768], P(None, 'col')
- residual: float32 [24, 32768], P(None, 'col')
The draws below stay inside these ranges and needn't reach their ends.
Inputs may be any that keep to these rules, and one draw needn't show every extreme that they name: Each of the 16 block rows appears exactly once in block_rows.
All inputs are finite; a program needn't handle non-finite values.
Results may differ from the reference program's by a relative error of at most 0.024.
Values may be sent and summed in bfloat16 or wider, within the bound.
No kernel may reach another device: no remote copies, remote signals or barrier semaphores. Data moves between devices by JAX's collectives and lax.ppermute only.
A program may use at most 128 MiB of HBM per device.

```python
import math
import jax
import jax.numpy as jnp
from jax import lax

BLK = 2048
NBLK = 16
RHS = 24
ITERS = 8
ORDER = 32768
RB = 2
CB = 1
N_ROW = 8
N_COL = 16


def draw_block_rows(key, part):
    order = jax.random.permutation(jax.random.fold_in(key, 11), NBLK)
    return order.astype(jnp.int32).reshape(-1, RB)


def draw_kernel_blocks(key, part):
    shape = (N_ROW, N_COL, RB, CB, BLK, BLK)
    scale = 1.0 / math.sqrt(8.0 * NBLK * BLK)
    values = jnp.clip(jax.random.normal(jax.random.fold_in(key, 5), shape, jnp.float32), -4.0, 4.0)
    return (values * scale).astype(jnp.bfloat16)


def block_levels(own_key, shape, shards, least, high):
    gain, own = 1.0, jax.random.fold_in(own_key, 6)
    for axis_at, parts in shards:
        heights = jnp.exp(jax.random.uniform(jax.random.fold_in(own, axis_at), (parts,), jnp.float32, least / len(shards), high / len(shards)))
        gain = gain * jnp.repeat(heights, shape[axis_at] // parts).reshape([-1 if axis == axis_at else 1 for axis in range(len(shape))])
    return gain


def gaussian(rng, dims, deviation, bound, shards=(), held_as=jnp.bfloat16):
    factor_of = block_levels(rng, dims, shards, -0.22, 0.18) if shards else 1.0
    array = jax.random.normal(rng, dims, jnp.float32) * deviation * factor_of
    return jnp.minimum(jnp.maximum(array, -bound), bound).astype(held_as)


def setup_inputs(seed: int = 0) -> dict:
    splits = jax.random.split(jax.random.key(seed), 5)
    return {
        "rhs": gaussian(splits[0], (RHS, ORDER), 1.0, 6.0, ((1, 16),), jnp.float32),
        "noise_var": jnp.clip(jnp.exp(math.log(3.6) - 1.3862944 * jax.random.uniform(splits[1], (ORDER,), jnp.float32) ** block_levels(splits[1], (ORDER,), ((0, 16),), -0.2, 0.2)), 0.9, 3.6),
        "block_rows": draw_block_rows(jax.random.fold_in(splits[4], 71), 0),
        "kernel_blocks": draw_kernel_blocks(jax.random.fold_in(splits[4], 71), 0),
    }


def reference(rhs, noise_var, block_rows, kernel_blocks):
    slot_total = N_ROW * N_COL * RB * CB
    row_ids = jnp.broadcast_to(block_rows[:, None, :, None], (N_ROW, N_COL, RB, CB)).reshape(slot_total).astype(jnp.int32)
    col_grid = jnp.arange(N_COL, dtype=jnp.int32)[:, None, None] * CB + jnp.arange(CB, dtype=jnp.int32)[None, None, :]
    col_ids = jnp.broadcast_to(col_grid[None], (N_ROW, N_COL, RB, CB)).reshape(slot_total).astype(jnp.int32)
    flat_blocks = kernel_blocks.reshape(slot_total, BLK, BLK)

    def operate(direction):
        dir_bf = direction.astype(jnp.bfloat16)

        def slot_step(image, item):
            block, row_id, col_id = item
            weight = (col_id >= row_id).astype(jnp.float32)
            row_start = (row_id * BLK).astype(jnp.int32)
            col_start = (col_id * BLK).astype(jnp.int32)
            col_piece = lax.dynamic_slice_in_dim(dir_bf, col_start, BLK, 1)
            row_piece = lax.dynamic_slice_in_dim(dir_bf, row_start, BLK, 1)
            forward = jnp.dot(col_piece, block.T, preferred_element_type=jnp.float32) * weight
            mirrored = jnp.dot(row_piece, block, preferred_element_type=jnp.float32) * weight
            current = lax.dynamic_slice_in_dim(image, row_start, BLK, 1)
            image = lax.dynamic_update_slice_in_dim(image, current + forward, row_start, 1)
            current = lax.dynamic_slice_in_dim(image, col_start, BLK, 1)
            image = lax.dynamic_update_slice_in_dim(image, current + mirrored, col_start, 1)
            return image, None

        image, _ = lax.scan(slot_step, noise_var[None, :] * direction, (flat_blocks, row_ids, col_ids))
        return image

    solution_field = jnp.zeros_like(rhs)
    residual = rhs
    direction = rhs
    norm_now = jnp.sum(residual * residual, axis=1)
    for step in range(ITERS):
        image = operate(direction)
        curvature = jnp.sum(direction * image, axis=1)
        alpha = norm_now / curvature
        solution_field = solution_field + alpha[:, None] * direction
        residual = residual - alpha[:, None] * image
        norm_next = jnp.sum(residual * residual, axis=1)
        direction = residual + (norm_next / norm_now)[:, None] * direction
        norm_now = norm_next
    return solution_field, residual
```

```python
import jax
import jax.numpy as jnp
from jax import lax
from jax.sharding import PartitionSpec as P

ITERS = 8
PAD = 8


def all_reduce(x, axis, n):
    rows, width = x.shape
    w = width // n
    y = lax.all_to_all(x.reshape(rows, n, w), axis, 1, 1, tiled=True)
    part = jnp.sum(y, axis=1)
    z = lax.all_to_all(jnp.broadcast_to(part[:, None, :], (rows, n, w)), axis, 1, 1, tiled=True)
    return z.reshape(rows, width)


def pack(blocks, scalars):
    width = blocks[0].shape[1]
    tail = jnp.zeros((PAD, width), jnp.float32).at[0, : scalars.shape[0]].set(scalars)
    return jnp.concatenate(list(blocks) + [tail], axis=0)


def make_on_device(n_row, n_col):
    def on_device(rhs, noise_var, block_rows, kernel_blocks):
        blocks = kernel_blocks[0, 0]
        rows = block_rows[0]
        nb = rows.shape[0]
        vecs, width = rhs.shape
        col = lax.axis_index("col")
        first_row = lax.axis_index("row") == 0
        used = [col >= rows[k] for k in range(nb)]
        owner = [col == rows[k] for k in range(nb)]
        noise = noise_var[None, :]

        def fetch(res):
            sent = [jnp.where(owner[k], res, 0.0) for k in range(nb)]
            out = all_reduce(pack(sent, jnp.sum(res * res, axis=1)), "col", n_col)
            return [out[k * vecs:(k + 1) * vecs] for k in range(nb)], out[nb * vecs, :vecs]

        solution = jnp.zeros_like(rhs)
        residual = rhs
        direction = rhs
        dir_rows, norm_now = fetch(rhs)
        for step in range(ITERS):
            vb = direction.astype(jnp.bfloat16)
            forward = []
            mirrored = jnp.zeros((vecs, width), jnp.float32)
            for k in range(nb):
                f = lax.dot_general(vb, blocks[k, 0], (((1,), (1,)), ((), ())), preferred_element_type=jnp.float32)
                forward.append(jnp.where(used[k], f, 0.0))
                m = jnp.dot(dir_rows[k].astype(jnp.bfloat16), blocks[k, 0], preferred_element_type=jnp.float32)
                mirrored = mirrored + jnp.where(used[k], m, 0.0)
            part = jnp.sum(direction * mirrored, axis=1)
            part = part + jnp.where(first_row, jnp.sum(direction * (noise * direction), axis=1), 0.0)
            for k in range(nb):
                part = part + jnp.sum(dir_rows[k] * forward[k], axis=1)
            out = all_reduce(pack(forward, part), "col", n_col)
            terms = mirrored
            for k in range(nb):
                terms = terms + jnp.where(owner[k], out[k * vecs:(k + 1) * vecs], 0.0)
            out = all_reduce(pack([terms], out[nb * vecs, :vecs]), "row", n_row)
            image = noise * direction + out[:vecs]
            curvature = out[vecs, :vecs]
            alpha = norm_now / curvature
            solution = solution + alpha[:, None] * direction
            residual = residual - alpha[:, None] * image
            if step + 1 < ITERS:
                res_rows, norm_next = fetch(residual)
                beta = norm_next / norm_now
                direction = residual + beta[:, None] * direction
                dir_rows = [res_rows[k] + beta[:, None] * dir_rows[k] for k in range(nb)]
                norm_now = norm_next
        return (solution, residual)

    return on_device


def solution(mesh):
    return jax.shard_map(
        make_on_device(mesh.shape["row"], mesh.shape["col"]),
        mesh=mesh,
        in_specs=(
            P(None, "col"),
            P("col"),
            P("row", None),
            P("row", "col", None, None, None, None),
        ),
        out_specs=(P(None, "col"), P(None, "col")),
        check_vma=False,
    )
```

```python
import jax
import jax.numpy as jnp
from jax import lax
from jax.experimental import pallas as pl
from jax.experimental.pallas import tpu as pltpu
from jax.sharding import PartitionSpec as P

ITERS = 8
PAD = 8


def all_reduce(x, axis, n):
    rows, width = x.shape
    w = width // n
    y = lax.all_to_all(x.reshape(rows, n, w), axis, 1, 1, tiled=True)
    part = jnp.sum(y, axis=1)
    z = lax.all_to_all(jnp.broadcast_to(part[:, None, :], (rows, n, w)), axis, 1, 1, tiled=True)
    return z.reshape(rows, width)


def products_kernel(vbc_ref, vbi_ref, k_ref, fwd_ref, m_ref):
    @pl.when((pl.program_id(0) == 0) & (pl.program_id(1) == 0))
    def _():
        m_ref[...] = jnp.zeros_like(m_ref)

    tile = k_ref[...]
    fwd_ref[...] = lax.dot_general(
        vbc_ref[...], tile, (((1,), (1,)), ((), ())), preferred_element_type=jnp.float32
    )
    m_ref[...] += jnp.dot(vbi_ref[...], tile, preferred_element_type=jnp.float32)


def block_products(vbc, vbi, blocks, tile=512):
    nb, _, order, _ = blocks.shape
    vecs = vbc.shape[0]
    return pl.pallas_call(
        products_kernel,
        grid=(nb, order // tile),
        in_specs=[
            pl.BlockSpec((vecs, order), lambda k, i: (0, 0)),
            pl.BlockSpec((None, vecs, tile), lambda k, i: (k, 0, i)),
            pl.BlockSpec((None, None, tile, order), lambda k, i: (k, 0, i, 0)),
        ],
        out_specs=[
            pl.BlockSpec((None, vecs, tile), lambda k, i: (k, 0, i)),
            pl.BlockSpec((vecs, order), lambda k, i: (0, 0)),
        ],
        out_shape=[
            jax.ShapeDtypeStruct((nb, vecs, order), jnp.float32),
            jax.ShapeDtypeStruct((vecs, order), jnp.float32),
        ],
        compiler_params=pltpu.CompilerParams(dimension_semantics=("arbitrary", "arbitrary")),
    )(vbc, vbi, blocks)


def pack(blocks, scalars):
    width = blocks[0].shape[1]
    tail = jnp.zeros((PAD, width), jnp.float32).at[0, : scalars.shape[0]].set(scalars)
    return jnp.concatenate(list(blocks) + [tail], axis=0)


def make_on_device(n_row, n_col):
    def on_device(rhs, noise_var, block_rows, kernel_blocks):
        blocks = kernel_blocks[0, 0]
        assert blocks.shape[1] == 1
        rows = block_rows[0]
        nb = rows.shape[0]
        vecs, width = rhs.shape
        col = lax.axis_index("col")
        first_row = lax.axis_index("row") == 0
        used = [col >= rows[k] for k in range(nb)]
        owner = [col == rows[k] for k in range(nb)]
        noise = noise_var[None, :]

        def fetch(res):
            sent = [jnp.where(owner[k], res, 0.0) for k in range(nb)]
            out = all_reduce(pack(sent, jnp.sum(res * res, axis=1)), "col", n_col)
            return [out[k * vecs:(k + 1) * vecs] for k in range(nb)], out[nb * vecs, :vecs]

        solution = jnp.zeros_like(rhs)
        residual = rhs
        direction = rhs
        dir_rows, norm_now = fetch(rhs)
        for step in range(ITERS):
            vb = direction.astype(jnp.bfloat16)
            vbi = jnp.stack([jnp.where(used[k], dir_rows[k], 0.0) for k in range(nb)]).astype(jnp.bfloat16)
            fwd, mirrored = block_products(vb, vbi, blocks)
            forward = [jnp.where(used[k], fwd[k], 0.0) for k in range(nb)]
            part = jnp.sum(direction * mirrored, axis=1)
            part = part + jnp.where(first_row, jnp.sum(direction * (noise * direction), axis=1), 0.0)
            for k in range(nb):
                part = part + jnp.sum(dir_rows[k] * forward[k], axis=1)
            out = all_reduce(pack(forward, part), "col", n_col)
            terms = mirrored
            for k in range(nb):
                terms = terms + jnp.where(owner[k], out[k * vecs:(k + 1) * vecs], 0.0)
            out = all_reduce(pack([terms], out[nb * vecs, :vecs]), "row", n_row)
            image = noise * direction + out[:vecs]
            curvature = out[vecs, :vecs]
            alpha = norm_now / curvature
            solution = solution + alpha[:, None] * direction
            residual = residual - alpha[:, None] * image
            if step + 1 < ITERS:
                res_rows, norm_next = fetch(residual)
                beta = norm_next / norm_now
                direction = residual + beta[:, None] * direction
                dir_rows = [res_rows[k] + beta[:, None] * dir_rows[k] for k in range(nb)]
                norm_now = norm_next
        return (solution, residual)

    return on_device


def solution(mesh):
    return jax.shard_map(
        make_on_device(mesh.shape["row"], mesh.shape["col"]),
        mesh=mesh,
        in_specs=(
            P(None, "col"),
            P("col"),
            P("row", None),
            P("row", "col", None, None, None, None),
        ),
        out_specs=(P(None, "col"), P(None, "col")),
        check_vma=False,
    )
```

```python
import jax
import jax.numpy as jnp
from jax import lax
from jax.experimental import pallas as pl
from jax.experimental.pallas import tpu as pltpu
from jax.sharding import PartitionSpec as P

ITERS = 8
PAD = 1


def all_reduce(x, axis, n):
    rows, width = x.shape
    w = width // n
    y = lax.all_to_all(x.reshape(rows, n, w), axis, 1, 1, tiled=True)
    part = jnp.sum(y, axis=1)
    z = lax.all_to_all(jnp.broadcast_to(part[:, None, :], (rows, n, w)), axis, 1, 1, tiled=True)
    return z.reshape(rows, width)


def products_kernel(vbc_ref, vbi_ref, k_ref, fwd_ref, m_ref):
    @pl.when((pl.program_id(0) == 0) & (pl.program_id(1) == 0))
    def _():
        m_ref[...] = jnp.zeros_like(m_ref)

    tile = k_ref[...]
    fwd_ref[...] = lax.dot_general(
        vbc_ref[...], tile, (((1,), (1,)), ((), ())), preferred_element_type=jnp.float32
    )
    m_ref[...] += jnp.dot(vbi_ref[...], tile, preferred_element_type=jnp.float32)


def block_products(vbc, vbi, blocks, tile=512):
    nb, _, order, _ = blocks.shape
    vecs = vbc.shape[0]
    return pl.pallas_call(
        products_kernel,
        grid=(nb, order // tile),
        in_specs=[
            pl.BlockSpec((vecs, order), lambda k, i: (0, 0)),
            pl.BlockSpec((None, vecs, tile), lambda k, i: (k, 0, i)),
            pl.BlockSpec((None, None, tile, order), lambda k, i: (k, 0, i, 0)),
        ],
        out_specs=[
            pl.BlockSpec((None, vecs, tile), lambda k, i: (k, 0, i)),
            pl.BlockSpec((vecs, order), lambda k, i: (0, 0)),
        ],
        out_shape=[
            jax.ShapeDtypeStruct((nb, vecs, order), jnp.float32),
            jax.ShapeDtypeStruct((vecs, order), jnp.float32),
        ],
        compiler_params=pltpu.CompilerParams(dimension_semantics=("arbitrary", "arbitrary")),
    )(vbc, vbi, blocks)


def pack(blocks, scalars):
    width = blocks[0].shape[1]
    tail = jnp.zeros((PAD, width), jnp.float32).at[0, : scalars.shape[0]].set(scalars)
    return jnp.concatenate(list(blocks) + [tail], axis=0)


def make_on_device(n_row, n_col):
    def on_device(rhs, noise_var, block_rows, kernel_blocks):
        blocks = kernel_blocks[0, 0]
        assert blocks.shape[1] == 1
        rows = block_rows[0]
        nb = rows.shape[0]
        vecs, width = rhs.shape
        col = lax.axis_index("col")
        first_row = lax.axis_index("row") == 0
        used = [col >= rows[k] for k in range(nb)]
        owner = [col == rows[k] for k in range(nb)]
        noise = noise_var[None, :]

        def fetch(res):
            sent = [jnp.where(owner[k], res, 0.0) for k in range(nb)]
            out = all_reduce(pack(sent, jnp.sum(res * res, axis=1)), "col", n_col)
            return [out[k * vecs:(k + 1) * vecs] for k in range(nb)], out[nb * vecs, :vecs]

        solution = jnp.zeros_like(rhs)
        residual = rhs
        direction = rhs
        dir_rows, norm_now = fetch(rhs)
        for step in range(ITERS):
            vb = direction.astype(jnp.bfloat16)
            vbi = jnp.stack([jnp.where(used[k], dir_rows[k], 0.0) for k in range(nb)]).astype(jnp.bfloat16)
            fwd, mirrored = block_products(vb, vbi, blocks)
            forward = [jnp.where(used[k], fwd[k], 0.0) for k in range(nb)]
            part = jnp.sum(direction * mirrored, axis=1)
            part = part + jnp.where(first_row, jnp.sum(direction * (noise * direction), axis=1), 0.0)
            for k in range(nb):
                part = part + jnp.sum(dir_rows[k] * forward[k], axis=1)
            out = all_reduce(pack(forward, part), "col", n_col)
            terms = mirrored
            for k in range(nb):
                terms = terms + jnp.where(owner[k], out[k * vecs:(k + 1) * vecs], 0.0)
            out = all_reduce(pack([terms], out[nb * vecs, :vecs]), "row", n_row)
            image = noise * direction + out[:vecs]
            curvature = out[vecs, :vecs]
            alpha = norm_now / curvature
            solution = solution + alpha[:, None] * direction
            residual = residual - alpha[:, None] * image
            if step + 1 < ITERS:
                res_rows, norm_next = fetch(residual)
                beta = norm_next / norm_now
                direction = residual + beta[:, None] * direction
                dir_rows = [res_rows[k] + beta[:, None] * dir_rows[k] for k in range(nb)]
                norm_now = norm_next
        return (solution, residual)

    return on_device


def solution(mesh):
    return jax.shard_map(
        make_on_device(mesh.shape["row"], mesh.shape["col"]),
        mesh=mesh,
        in_specs=(
            P(None, "col"),
            P("col"),
            P("row", None),
            P("row", "col", None, None, None, None),
        ),
        out_specs=(P(None, "col"), P(None, "col")),
        check_vma=False,
    )
```

```python
import jax
import jax.numpy as jnp
from jax import lax
from jax.experimental import pallas as pl
from jax.experimental.pallas import tpu as pltpu
from jax.sharding import PartitionSpec as P

ITERS = 8
PAD = 8


def all_reduce(x, axis, n, late=None):
    rows, width = x.shape
    w = width // n
    y = lax.all_to_all(x.reshape(rows, n, w), axis, 1, 1, tiled=True)
    part = jnp.sum(y, axis=1)
    if late is not None:
        extra = jnp.zeros((PAD, w), jnp.float32).at[0, : late.shape[0]].set(late)
        part = jnp.concatenate([part, extra], axis=0)
    z = lax.all_to_all(jnp.broadcast_to(part[:, None, :], part.shape[:1] + (n, w)), axis, 1, 1, tiled=True)
    if late is None:
        return z.reshape(rows, width), None
    lates = z[rows, :, : late.shape[0]]
    return z[:rows].reshape(rows, width), jnp.sum(lates, axis=0)


def forward_kernel(vbc_ref, k_ref, fwd_ref):
    fwd_ref[...] = lax.dot_general(
        vbc_ref[...], k_ref[...], (((1,), (1,)), ((), ())), preferred_element_type=jnp.float32
    )


def mirrored_kernel(vbi_ref, k_ref, m_ref):
    @pl.when((pl.program_id(0) == 0) & (pl.program_id(1) == 0))
    def _():
        m_ref[...] = jnp.zeros_like(m_ref)

    m_ref[...] += jnp.dot(vbi_ref[...], k_ref[...], preferred_element_type=jnp.float32)


def forward_products(vbc, blocks, tile=512):
    nb, _, order, _ = blocks.shape
    vecs = vbc.shape[0]
    return pl.pallas_call(
        forward_kernel,
        grid=(nb, order // tile),
        in_specs=[
            pl.BlockSpec((vecs, order), lambda k, i: (0, 0)),
            pl.BlockSpec((None, None, tile, order), lambda k, i: (k, 0, i, 0)),
        ],
        out_specs=pl.BlockSpec((None, vecs, tile), lambda k, i: (k, 0, i)),
        out_shape=jax.ShapeDtypeStruct((nb, vecs, order), jnp.float32),
        compiler_params=pltpu.CompilerParams(dimension_semantics=("arbitrary", "arbitrary")),
    )(vbc, blocks)


def mirrored_products(vbi, blocks, tile=512):
    nb, _, order, _ = blocks.shape
    vecs = vbi.shape[1]
    return pl.pallas_call(
        mirrored_kernel,
        grid=(nb, order // tile),
        in_specs=[
            pl.BlockSpec((None, vecs, tile), lambda k, i: (k, 0, i)),
            pl.BlockSpec((None, None, tile, order), lambda k, i: (k, 0, i, 0)),
        ],
        out_specs=pl.BlockSpec((vecs, order), lambda k, i: (0, 0)),
        out_shape=jax.ShapeDtypeStruct((vecs, order), jnp.float32),
        compiler_params=pltpu.CompilerParams(dimension_semantics=("arbitrary", "arbitrary")),
    )(vbi, blocks)


def pack(blocks, scalars):
    width = blocks[0].shape[1]
    tail = jnp.zeros((PAD, width), jnp.float32).at[0, : scalars.shape[0]].set(scalars)
    return jnp.concatenate(list(blocks) + [tail], axis=0)


def make_on_device(n_row, n_col):
    def on_device(rhs, noise_var, block_rows, kernel_blocks):
        blocks = kernel_blocks[0, 0]
        assert blocks.shape[1] == 1
        rows = block_rows[0]
        nb = rows.shape[0]
        vecs, width = rhs.shape
        col = lax.axis_index("col")
        first_row = lax.axis_index("row") == 0
        used = [col >= rows[k] for k in range(nb)]
        owner = [col == rows[k] for k in range(nb)]
        noise = noise_var[None, :]

        def fetch(res):
            sent = [jnp.where(owner[k], res, 0.0) for k in range(nb)]
            out, _ = all_reduce(pack(sent, jnp.sum(res * res, axis=1)), "col", n_col)
            return [out[k * vecs:(k + 1) * vecs] for k in range(nb)], out[nb * vecs, :vecs]

        solution = jnp.zeros_like(rhs)
        residual = rhs
        direction = rhs
        dir_rows, norm_now = fetch(rhs)
        for step in range(ITERS):
            vb = direction.astype(jnp.bfloat16)
            fwd = forward_products(vb, blocks)
            forward = [jnp.where(used[k], fwd[k], 0.0) for k in range(nb)]
            part = jnp.where(first_row, jnp.sum(direction * (noise * direction), axis=1), 0.0)
            for k in range(nb):
                part = part + jnp.sum(dir_rows[k] * forward[k], axis=1)
            vbi = jnp.stack([jnp.where(used[k], dir_rows[k], 0.0) for k in range(nb)]).astype(jnp.bfloat16)
            mirrored = mirrored_products(vbi, blocks)
            out, late = all_reduce(pack(forward, part), "col", n_col, late=jnp.sum(direction * mirrored, axis=1))
            terms = mirrored
            for k in range(nb):
                terms = terms + jnp.where(owner[k], out[k * vecs:(k + 1) * vecs], 0.0)
            out, _ = all_reduce(pack([terms], out[nb * vecs, :vecs] + late), "row", n_row)
            image = noise * direction + out[:vecs]
            curvature = out[vecs, :vecs]
            alpha = norm_now / curvature
            solution = solution + alpha[:, None] * direction
            residual = residual - alpha[:, None] * image
            if step + 1 < ITERS:
                res_rows, norm_next = fetch(residual)
                beta = norm_next / norm_now
                direction = residual + beta[:, None] * direction
                dir_rows = [res_rows[k] + beta[:, None] * dir_rows[k] for k in range(nb)]
                norm_now = norm_next
        return (solution, residual)

    return on_device


def solution(mesh):
    return jax.shard_map(
        make_on_device(mesh.shape["row"], mesh.shape["col"]),
        mesh=mesh,
        in_specs=(
            P(None, "col"),
            P("col"),
            P("row", None),
            P("row", "col", None, None, None, None),
        ),
        out_specs=(P(None, "col"), P(None, "col")),
        check_vma=False,
    )
```

```python
import jax
import jax.numpy as jnp
from jax import lax
from jax.experimental import pallas as pl
from jax.experimental.pallas import tpu as pltpu
from jax.sharding import PartitionSpec as P

ITERS = 8
PAD = 8


def all_reduce(x, axis, n):
    rows, width = x.shape
    w = width // n
    y = lax.all_to_all(x.reshape(rows, n, w), axis, 1, 1, tiled=True)
    part = jnp.sum(y, axis=1)
    z = lax.all_to_all(jnp.broadcast_to(part[:, None, :], (rows, n, w)), axis, 1, 1, tiled=True)
    return z.reshape(rows, width)


def products_kernel(flags_ref, d_ref, di_ref, k_ref, fwd_ref, m_ref, p_ref):
    k = pl.program_id(0)
    i = pl.program_id(1)

    @pl.when((k == 0) & (i == 0))
    def _():
        m_ref[...] = jnp.zeros_like(m_ref)
        p_ref[...] = jnp.zeros_like(p_ref)

    used = flags_ref[k] != 0
    tile = k_ref[...]
    f = lax.dot_general(
        d_ref[...].astype(jnp.bfloat16), tile, (((1,), (1,)), ((), ())), preferred_element_type=jnp.float32
    )
    f = jnp.where(used, f, 0.0)
    fwd_ref[...] = f
    di = di_ref[...]
    acc = p_ref[...]
    for j in range(f.shape[1] // 128):
        acc = acc + di[:, j * 128:(j + 1) * 128] * f[:, j * 128:(j + 1) * 128]
    p_ref[...] = acc
    vbi = jnp.where(used, di, 0.0).astype(jnp.bfloat16)
    m_ref[...] += jnp.dot(vbi, tile, preferred_element_type=jnp.float32)

    @pl.when((k == pl.num_programs(0) - 1) & (i == pl.num_programs(1) - 1))
    def _():
        acc = p_ref[...]
        for j in range(m_ref.shape[1] // 128):
            acc = acc + d_ref[:, j * 128:(j + 1) * 128] * m_ref[:, j * 128:(j + 1) * 128]
        p_ref[...] = acc


def block_products(flags, d, di, blocks, tile=512):
    nb, _, order, _ = blocks.shape
    vecs = d.shape[0]
    grid_spec = pltpu.PrefetchScalarGridSpec(
        num_scalar_prefetch=1,
        grid=(nb, order // tile),
        in_specs=[
            pl.BlockSpec((vecs, order), lambda k, i, f: (0, 0)),
            pl.BlockSpec((None, vecs, tile), lambda k, i, f: (k, 0, i)),
            pl.BlockSpec((None, None, tile, order), lambda k, i, f: (k, 0, i, 0)),
        ],
        out_specs=[
            pl.BlockSpec((None, vecs, tile), lambda k, i, f: (k, 0, i)),
            pl.BlockSpec((vecs, order), lambda k, i, f: (0, 0)),
            pl.BlockSpec((vecs, 128), lambda k, i, f: (0, 0)),
        ],
    )
    return pl.pallas_call(
        products_kernel,
        grid_spec=grid_spec,
        out_shape=[
            jax.ShapeDtypeStruct((nb, vecs, order), jnp.float32),
            jax.ShapeDtypeStruct((vecs, order), jnp.float32),
            jax.ShapeDtypeStruct((vecs, 128), jnp.float32),
        ],
        compiler_params=pltpu.CompilerParams(dimension_semantics=("arbitrary", "arbitrary")),
    )(flags, d, di, blocks)


def pack(blocks, scalars):
    width = blocks[0].shape[1]
    tail = jnp.zeros((PAD, width), jnp.float32).at[0, : scalars.shape[0]].set(scalars)
    return jnp.concatenate(list(blocks) + [tail], axis=0)


def make_on_device(n_row, n_col):
    def on_device(rhs, noise_var, block_rows, kernel_blocks):
        blocks = kernel_blocks[0, 0]
        assert blocks.shape[1] == 1
        rows = block_rows[0]
        nb = rows.shape[0]
        vecs, width = rhs.shape
        col = lax.axis_index("col")
        first_row = lax.axis_index("row") == 0
        flags = (col >= rows).astype(jnp.int32)
        owner = [col == rows[k] for k in range(nb)]
        noise = noise_var[None, :]

        def fetch(res):
            sent = [jnp.where(owner[k], res, 0.0) for k in range(nb)]
            out = all_reduce(pack(sent, jnp.sum(res * res, axis=1)), "col", n_col)
            return out[: nb * vecs].reshape(nb, vecs, width), out[nb * vecs, :vecs]

        solution = jnp.zeros_like(rhs)
        residual = rhs
        direction = rhs
        dir_rows, norm_now = fetch(rhs)
        for step in range(ITERS):
            fwd, mirrored, lanes = block_products(flags, direction, dir_rows, blocks)
            forward = [fwd[k] for k in range(nb)]
            part = jnp.sum(lanes, axis=1)
            part = part + jnp.where(first_row, jnp.sum(direction * (noise * direction), axis=1), 0.0)
            out = all_reduce(pack(forward, part), "col", n_col)
            terms = mirrored
            for k in range(nb):
                terms = terms + jnp.where(owner[k], out[k * vecs:(k + 1) * vecs], 0.0)
            out = all_reduce(pack([terms], out[nb * vecs, :vecs]), "row", n_row)
            image = noise * direction + out[:vecs]
            curvature = out[vecs, :vecs]
            alpha = norm_now / curvature
            solution = solution + alpha[:, None] * direction
            residual = residual - alpha[:, None] * image
            if step + 1 < ITERS:
                res_rows, norm_next = fetch(residual)
                beta = norm_next / norm_now
                direction = residual + beta[:, None] * direction
                dir_rows = res_rows + beta[None, :, None] * dir_rows
                norm_now = norm_next
        return (solution, residual)

    return on_device


def solution(mesh):
    return jax.shard_map(
        make_on_device(mesh.shape["row"], mesh.shape["col"]),
        mesh=mesh,
        in_specs=(
            P(None, "col"),
            P("col"),
            P("row", None),
            P("row", "col", None, None, None, None),
        ),
        out_specs=(P(None, "col"), P(None, "col")),
        check_vma=False,
    )
```

```python
import jax
import jax.numpy as jnp
from jax import lax
from jax.experimental import pallas as pl
from jax.experimental.pallas import tpu as pltpu
from jax.sharding import PartitionSpec as P

ITERS = 8
PAD = 8


def all_reduce(x, axis, n):
    rows, width = x.shape
    w = width // n
    y = lax.all_to_all(x.reshape(rows, n, w), axis, 1, 1, tiled=True)
    part = jnp.sum(y, axis=1)
    z = lax.all_to_all(jnp.broadcast_to(part[:, None, :], (rows, n, w)), axis, 1, 1, tiled=True)
    return z.reshape(rows, width)


def products_kernel(flags_ref, d_ref, di_ref, k_ref, fwd_ref, m_ref, p_ref):
    k = pl.program_id(0)
    i = pl.program_id(1)

    @pl.when((k == 0) & (i == 0))
    def _():
        m_ref[...] = jnp.zeros_like(m_ref)
        p_ref[...] = jnp.zeros_like(p_ref)

    used = flags_ref[k] != 0
    tile = k_ref[...]
    f = lax.dot_general(
        d_ref[...].astype(jnp.bfloat16), tile, (((1,), (1,)), ((), ())), preferred_element_type=jnp.float32
    )
    f = jnp.where(used, f, 0.0)
    fwd_ref[...] = f
    di = di_ref[...]
    acc = p_ref[...]
    for j in range(f.shape[1] // 128):
        acc = acc + di[:, j * 128:(j + 1) * 128] * f[:, j * 128:(j + 1) * 128]
    p_ref[...] = acc
    vbi = jnp.where(used, di, 0.0).astype(jnp.bfloat16)
    m_ref[...] += jnp.dot(vbi, tile, preferred_element_type=jnp.float32)

    @pl.when((k == pl.num_programs(0) - 1) & (i == pl.num_programs(1) - 1))
    def _():
        acc = p_ref[...]
        for j in range(m_ref.shape[1] // 128):
            acc = acc + d_ref[:, j * 128:(j + 1) * 128] * m_ref[:, j * 128:(j + 1) * 128]
        p_ref[...] = acc


def block_products(flags, d, di, blocks, tile=512):
    nb, _, order, _ = blocks.shape
    vecs = d.shape[0]
    grid_spec = pltpu.PrefetchScalarGridSpec(
        num_scalar_prefetch=1,
        grid=(nb, order // tile),
        in_specs=[
            pl.BlockSpec((vecs, order), lambda k, i, f: (0, 0)),
            pl.BlockSpec((None, vecs, tile), lambda k, i, f: (k, 0, i)),
            pl.BlockSpec((None, None, tile, order), lambda k, i, f: (k, 0, i, 0)),
        ],
        out_specs=[
            pl.BlockSpec((None, vecs, tile), lambda k, i, f: (k, 0, i)),
            pl.BlockSpec((vecs, order), lambda k, i, f: (0, 0)),
            pl.BlockSpec((vecs, 128), lambda k, i, f: (0, 0)),
        ],
    )
    return pl.pallas_call(
        products_kernel,
        grid_spec=grid_spec,
        out_shape=[
            jax.ShapeDtypeStruct((nb, vecs, order), jnp.float32),
            jax.ShapeDtypeStruct((vecs, order), jnp.float32),
            jax.ShapeDtypeStruct((vecs, 128), jnp.float32),
        ],
        compiler_params=pltpu.CompilerParams(dimension_semantics=("arbitrary", "arbitrary")),
    )(flags, d, di, blocks)


def pack(blocks, scalars):
    width = blocks[0].shape[1]
    tail = jnp.zeros((PAD, width), jnp.float32).at[0, : scalars.shape[0]].set(scalars)
    return jnp.concatenate(list(blocks) + [tail], axis=0)


def make_on_device(n_row, n_col):
    def on_device(rhs, noise_var, block_rows, kernel_blocks):
        blocks = kernel_blocks[0, 0]
        assert blocks.shape[1] == 1
        rows = block_rows[0]
        nb = rows.shape[0]
        vecs, width = rhs.shape
        col = lax.axis_index("col")
        first_row = lax.axis_index("row") == 0
        flags = (col >= rows).astype(jnp.int32)
        owner = [col == rows[k] for k in range(nb)]
        noise = noise_var[None, :]

        def fetch(res):
            w = width // n_col
            tail = jnp.zeros((PAD, n_col, w), jnp.float32).at[0, :, :vecs].set(
                jnp.broadcast_to(jnp.sum(res * res, axis=1), (n_col, vecs))
            )
            x = jnp.concatenate([res.reshape(vecs, n_col, w), tail], axis=0)
            y = lax.all_to_all(x, "col", 1, 1, tiled=True)
            norm = jnp.sum(y[vecs, :, :vecs], axis=0)
            kept = jnp.concatenate(
                [lax.dynamic_index_in_dim(y[:vecs], rows[k], axis=1, keepdims=False) for k in range(nb)], axis=0
            )
            z = lax.all_to_all(jnp.broadcast_to(kept[:, None, :], (nb * vecs, n_col, w)), "col", 1, 1, tiled=True)
            return z.reshape(nb, vecs, width), norm

        solution = jnp.zeros_like(rhs)
        residual = rhs
        direction = rhs
        dir_rows, norm_now = fetch(rhs)
        for step in range(ITERS):
            fwd, mirrored, lanes = block_products(flags, direction, dir_rows, blocks)
            forward = [fwd[k] for k in range(nb)]
            part = jnp.sum(lanes, axis=1)
            part = part + jnp.where(first_row, jnp.sum(direction * (noise * direction), axis=1), 0.0)
            out = all_reduce(pack(forward, part), "col", n_col)
            terms = mirrored
            for k in range(nb):
                terms = terms + jnp.where(owner[k], out[k * vecs:(k + 1) * vecs], 0.0)
            out = all_reduce(pack([terms], out[nb * vecs, :vecs]), "row", n_row)
            image = noise * direction + out[:vecs]
            curvature = out[vecs, :vecs]
            alpha = norm_now / curvature
            solution = solution + alpha[:, None] * direction
            residual = residual - alpha[:, None] * image
            if step + 1 < ITERS:
                res_rows, norm_next = fetch(residual)
                beta = norm_next / norm_now
                direction = residual + beta[:, None] * direction
                dir_rows = res_rows + beta[None, :, None] * dir_rows
                norm_now = norm_next
        return (solution, residual)

    return on_device


def solution(mesh):
    return jax.shard_map(
        make_on_device(mesh.shape["row"], mesh.shape["col"]),
        mesh=mesh,
        in_specs=(
            P(None, "col"),
            P("col"),
            P("row", None),
            P("row", "col", None, None, None, None),
        ),
        out_specs=(P(None, "col"), P(None, "col")),
        check_vma=False,
    )
```

```python
import jax
import jax.numpy as jnp
from jax import lax
from jax.experimental import pallas as pl
from jax.experimental.pallas import tpu as pltpu
from jax.sharding import PartitionSpec as P

ITERS = 8
PAD = 8


def all_reduce(x, axis, n):
    rows, width = x.shape
    w = width // n
    y = lax.all_to_all(x.reshape(rows, n, w), axis, 1, 1, tiled=True)
    part = jnp.sum(y, axis=1)
    z = lax.all_to_all(jnp.broadcast_to(part[:, None, :], (rows, n, w)), axis, 1, 1, tiled=True)
    return z.reshape(rows, width)


def products_kernel(flags_ref, d_ref, di_ref, k_ref, fwd_ref, m_ref, p_ref):
    k = pl.program_id(0)
    i = pl.program_id(1)

    @pl.when((k == 0) & (i == 0))
    def _():
        m_ref[...] = jnp.zeros_like(m_ref)
        p_ref[...] = jnp.zeros_like(p_ref)

    used = flags_ref[k] != 0
    tile = k_ref[...]
    f = lax.dot_general(
        d_ref[...].astype(jnp.bfloat16), tile, (((1,), (1,)), ((), ())), preferred_element_type=jnp.float32
    )
    f = jnp.where(used, f, 0.0)
    fwd_ref[...] = f
    di = di_ref[...]
    acc = p_ref[...]
    for j in range(f.shape[1] // 128):
        acc = acc + di[:, j * 128:(j + 1) * 128] * f[:, j * 128:(j + 1) * 128]
    p_ref[...] = acc
    vbi = jnp.where(used, di, 0.0).astype(jnp.bfloat16)
    m_ref[...] += jnp.dot(vbi, tile, preferred_element_type=jnp.float32)

    @pl.when((k == pl.num_programs(0) - 1) & (i == pl.num_programs(1) - 1))
    def _():
        acc = p_ref[...]
        for j in range(m_ref.shape[1] // 128):
            acc = acc + d_ref[:, j * 128:(j + 1) * 128] * m_ref[:, j * 128:(j + 1) * 128]
        p_ref[...] = acc


def block_products(flags, d, di, blocks, tile=512):
    nb, _, order, _ = blocks.shape
    vecs = d.shape[0]
    grid_spec = pltpu.PrefetchScalarGridSpec(
        num_scalar_prefetch=1,
        grid=(nb, order // tile),
        in_specs=[
            pl.BlockSpec((vecs, order), lambda k, i, f: (0, 0)),
            pl.BlockSpec((None, vecs, tile), lambda k, i, f: (k, 0, i)),
            pl.BlockSpec((None, None, tile, order), lambda k, i, f: (k, 0, i, 0)),
        ],
        out_specs=[
            pl.BlockSpec((None, vecs, tile), lambda k, i, f: (k, 0, i)),
            pl.BlockSpec((vecs, order), lambda k, i, f: (0, 0)),
            pl.BlockSpec((vecs, 128), lambda k, i, f: (0, 0)),
        ],
    )
    return pl.pallas_call(
        products_kernel,
        grid_spec=grid_spec,
        out_shape=[
            jax.ShapeDtypeStruct((nb, vecs, order), jnp.float32),
            jax.ShapeDtypeStruct((vecs, order), jnp.float32),
            jax.ShapeDtypeStruct((vecs, 128), jnp.float32),
        ],
        compiler_params=pltpu.CompilerParams(dimension_semantics=("arbitrary", "arbitrary")),
    )(flags, d, di, blocks)


def scalar_tail(scalars, n, w):
    return jnp.zeros((PAD, n, w), jnp.float32).at[0, :, : scalars.shape[0]].set(
        jnp.broadcast_to(scalars, (n, scalars.shape[0]))
    )


def pack(blocks, scalars):
    width = blocks[0].shape[1]
    tail = jnp.zeros((PAD, width), jnp.float32).at[0, : scalars.shape[0]].set(scalars)
    return jnp.concatenate(list(blocks) + [tail], axis=0)


def make_on_device(n_row, n_col):
    def on_device(rhs, noise_var, block_rows, kernel_blocks):
        blocks = kernel_blocks[0, 0]
        assert blocks.shape[1] == 1
        rows = block_rows[0]
        nb = rows.shape[0]
        vecs, width = rhs.shape
        col = lax.axis_index("col")
        first_row = lax.axis_index("row") == 0
        flags = (col >= rows).astype(jnp.int32)
        noise = noise_var[None, :]

        def fetch(res):
            w = width // n_col
            x = jnp.concatenate([res.reshape(vecs, n_col, w), scalar_tail(jnp.sum(res * res, axis=1), n_col, w)], axis=0)
            y = lax.all_to_all(x, "col", 1, 1, tiled=True)
            norm = jnp.sum(y[vecs, :, :vecs], axis=0)
            kept = jnp.concatenate(
                [lax.dynamic_index_in_dim(y[:vecs], rows[k], axis=1, keepdims=False) for k in range(nb)], axis=0
            )
            z = lax.all_to_all(jnp.broadcast_to(kept[:, None, :], (nb * vecs, n_col, w)), "col", 1, 1, tiled=True)
            return z.reshape(nb, vecs, width), norm

        solution = jnp.zeros_like(rhs)
        residual = rhs
        direction = rhs
        dir_rows, norm_now = fetch(rhs)
        for step in range(ITERS):
            fwd, mirrored, lanes = block_products(flags, direction, dir_rows, blocks)
            forward = [fwd[k] for k in range(nb)]
            part = jnp.sum(lanes, axis=1)
            part = part + jnp.where(first_row, jnp.sum(direction * (noise * direction), axis=1), 0.0)
            w = width // n_col
            x = jnp.concatenate([fwd.reshape(nb * vecs, n_col, w), scalar_tail(part, n_col, w)], axis=0)
            s = jnp.sum(lax.all_to_all(x, "col", 1, 1, tiled=True), axis=1)
            chunks = s[: nb * vecs].reshape(nb, vecs, w)
            dest = jnp.arange(n_col, dtype=jnp.int32)[None, :, None]
            send = jnp.zeros((vecs, n_col, w), jnp.float32)
            for k in range(nb):
                send = jnp.where(dest == rows[k], chunks[k][:, None, :], send)
            owned = lax.all_to_all(send, "col", 1, 1, tiled=True).reshape(vecs, width)
            terms = mirrored + owned
            w = width // n_row
            x = jnp.concatenate([terms.reshape(vecs, n_row, w), scalar_tail(s[nb * vecs, :vecs], n_row, w)], axis=0)
            s = jnp.sum(lax.all_to_all(x, "row", 1, 1, tiled=True), axis=1)
            curvature = s[vecs, :vecs]
            kernel_part = lax.all_to_all(
                jnp.broadcast_to(s[:vecs][:, None, :], (vecs, n_row, w)), "row", 1, 1, tiled=True
            ).reshape(vecs, width)
            image = noise * direction + kernel_part
            alpha = norm_now / curvature
            solution = solution + alpha[:, None] * direction
            residual = residual - alpha[:, None] * image
            if step + 1 < ITERS:
                res_rows, norm_next = fetch(residual)
                beta = norm_next / norm_now
                direction = residual + beta[:, None] * direction
                dir_rows = res_rows + beta[None, :, None] * dir_rows
                norm_now = norm_next
        return (solution, residual)

    return on_device


def solution(mesh):
    return jax.shard_map(
        make_on_device(mesh.shape["row"], mesh.shape["col"]),
        mesh=mesh,
        in_specs=(
            P(None, "col"),
            P("col"),
            P("row", None),
            P("row", "col", None, None, None, None),
        ),
        out_specs=(P(None, "col"), P(None, "col")),
        check_vma=False,
    )
```

```python
import jax
import jax.numpy as jnp
from jax import lax
from jax.experimental import pallas as pl
from jax.experimental.pallas import tpu as pltpu
from jax.sharding import PartitionSpec as P

ITERS = 8
PAD = 8


def all_reduce(x, axis, n):
    rows, width = x.shape
    w = width // n
    y = lax.all_to_all(x.reshape(rows, n, w), axis, 1, 1, tiled=True)
    part = jnp.sum(y, axis=1)
    z = lax.all_to_all(jnp.broadcast_to(part[:, None, :], (rows, n, w)), axis, 1, 1, tiled=True)
    return z.reshape(rows, width)


def products_kernel(flags_ref, d_ref, di_ref, k_ref, fwd_ref, m_ref, p_ref):
    k = pl.program_id(0)
    i = pl.program_id(1)

    @pl.when((k == 0) & (i == 0))
    def _():
        m_ref[...] = jnp.zeros_like(m_ref)
        p_ref[...] = jnp.zeros_like(p_ref)

    used = flags_ref[k] != 0
    tile = k_ref[...]
    f = lax.dot_general(
        d_ref[...].astype(jnp.bfloat16), tile, (((1,), (1,)), ((), ())), preferred_element_type=jnp.float32
    )
    f = jnp.where(used, f, 0.0)
    fwd_ref[...] = f
    di = di_ref[...]
    acc = p_ref[...]
    for j in range(f.shape[1] // 128):
        acc = acc + di[:, j * 128:(j + 1) * 128] * f[:, j * 128:(j + 1) * 128]
    p_ref[...] = acc
    vbi = jnp.where(used, di, 0.0).astype(jnp.bfloat16)
    m_ref[...] += jnp.dot(vbi, tile, preferred_element_type=jnp.float32)

    @pl.when((k == pl.num_programs(0) - 1) & (i == pl.num_programs(1) - 1))
    def _():
        acc = p_ref[...]
        for j in range(m_ref.shape[1] // 128):
            acc = acc + d_ref[:, j * 128:(j + 1) * 128] * m_ref[:, j * 128:(j + 1) * 128]
        p_ref[...] = acc


def block_products(flags, d, di, blocks, tile=1024):
    nb, _, order, _ = blocks.shape
    vecs = d.shape[0]
    grid_spec = pltpu.PrefetchScalarGridSpec(
        num_scalar_prefetch=1,
        grid=(nb, order // tile),
        in_specs=[
            pl.BlockSpec((vecs, order), lambda k, i, f: (0, 0)),
            pl.BlockSpec((None, vecs, tile), lambda k, i, f: (k, 0, i)),
            pl.BlockSpec((None, None, tile, order), lambda k, i, f: (k, 0, i, 0)),
        ],
        out_specs=[
            pl.BlockSpec((None, vecs, tile), lambda k, i, f: (k, 0, i)),
            pl.BlockSpec((vecs, order), lambda k, i, f: (0, 0)),
            pl.BlockSpec((vecs, 128), lambda k, i, f: (0, 0)),
        ],
    )
    return pl.pallas_call(
        products_kernel,
        grid_spec=grid_spec,
        out_shape=[
            jax.ShapeDtypeStruct((nb, vecs, order), jnp.float32),
            jax.ShapeDtypeStruct((vecs, order), jnp.float32),
            jax.ShapeDtypeStruct((vecs, 128), jnp.float32),
        ],
        compiler_params=pltpu.CompilerParams(dimension_semantics=("arbitrary", "arbitrary")),
    )(flags, d, di, blocks)


def pack(blocks, scalars):
    width = blocks[0].shape[1]
    tail = jnp.zeros((PAD, width), jnp.float32).at[0, : scalars.shape[0]].set(scalars)
    return jnp.concatenate(list(blocks) + [tail], axis=0)


def make_on_device(n_row, n_col):
    def on_device(rhs, noise_var, block_rows, kernel_blocks):
        blocks = kernel_blocks[0, 0]
        assert blocks.shape[1] == 1
        rows = block_rows[0]
        nb = rows.shape[0]
        vecs, width = rhs.shape
        col = lax.axis_index("col")
        first_row = lax.axis_index("row") == 0
        flags = (col >= rows).astype(jnp.int32)
        owner = [col == rows[k] for k in range(nb)]
        noise = noise_var[None, :]

        def fetch(res):
            w = width // n_col
            tail = jnp.zeros((PAD, n_col, w), jnp.float32).at[0, :, :vecs].set(
                jnp.broadcast_to(jnp.sum(res * res, axis=1), (n_col, vecs))
            )
            x = jnp.concatenate([res.reshape(vecs, n_col, w), tail], axis=0)
            y = lax.all_to_all(x, "col", 1, 1, tiled=True)
            norm = jnp.sum(y[vecs, :, :vecs], axis=0)
            kept = jnp.concatenate(
                [lax.dynamic_index_in_dim(y[:vecs], rows[k], axis=1, keepdims=False) for k in range(nb)], axis=0
            )
            z = lax.all_to_all(jnp.broadcast_to(kept[:, None, :], (nb * vecs, n_col, w)), "col", 1, 1, tiled=True)
            return z.reshape(nb, vecs, width), norm

        solution = jnp.zeros_like(rhs)
        residual = rhs
        direction = rhs
        dir_rows, norm_now = fetch(rhs)
        for step in range(ITERS):
            fwd, mirrored, lanes = block_products(flags, direction, dir_rows, blocks)
            forward = [fwd[k] for k in range(nb)]
            part = jnp.sum(lanes, axis=1)
            part = part + jnp.where(first_row, jnp.sum(direction * (noise * direction), axis=1), 0.0)
            out = all_reduce(pack(forward, part), "col", n_col)
            terms = mirrored
            for k in range(nb):
                terms = terms + jnp.where(owner[k], out[k * vecs:(k + 1) * vecs], 0.0)
            out = all_reduce(pack([terms], out[nb * vecs, :vecs]), "row", n_row)
            image = noise * direction + out[:vecs]
            curvature = out[vecs, :vecs]
            alpha = norm_now / curvature
            solution = solution + alpha[:, None] * direction
            residual = residual - alpha[:, None] * image
            if step + 1 < ITERS:
                res_rows, norm_next = fetch(residual)
                beta = norm_next / norm_now
                direction = residual + beta[:, None] * direction
                dir_rows = res_rows + beta[None, :, None] * dir_rows
                norm_now = norm_next
        return (solution, residual)

    return on_device


def solution(mesh):
    return jax.shard_map(
        make_on_device(mesh.shape["row"], mesh.shape["col"]),
        mesh=mesh,
        in_specs=(
            P(None, "col"),
            P("col"),
            P("row", None),
            P("row", "col", None, None, None, None),
        ),
        out_specs=(P(None, "col"), P(None, "col")),
        check_vma=False,
    )
```

```python
import jax
import jax.numpy as jnp
from jax import lax
from jax.experimental import pallas as pl
from jax.experimental.pallas import tpu as pltpu
from jax.sharding import PartitionSpec as P

ITERS = 8
PAD = 8


def all_reduce(x, axis, n):
    rows, width = x.shape
    w = width // n
    y = lax.all_to_all(x, axis, 1, 1, tiled=True)
    part = jnp.sum(y.reshape(rows, n, w), axis=1)
    return lax.all_to_all(jnp.tile(part, (1, n)), axis, 1, 1, tiled=True)


def products_kernel(flags_ref, d_ref, di_ref, k_ref, fwd_ref, m_ref, p_ref):
    k = pl.program_id(0)
    i = pl.program_id(1)

    @pl.when((k == 0) & (i == 0))
    def _():
        m_ref[...] = jnp.zeros_like(m_ref)
        p_ref[...] = jnp.zeros_like(p_ref)

    used = flags_ref[k] != 0
    tile = k_ref[...]
    f = lax.dot_general(
        d_ref[...].astype(jnp.bfloat16), tile, (((1,), (1,)), ((), ())), preferred_element_type=jnp.float32
    )
    f = jnp.where(used, f, 0.0)
    fwd_ref[...] = f
    di = di_ref[...]
    acc = p_ref[...]
    for j in range(f.shape[1] // 128):
        acc = acc + di[:, j * 128:(j + 1) * 128] * f[:, j * 128:(j + 1) * 128]
    p_ref[...] = acc
    vbi = jnp.where(used, di, 0.0).astype(jnp.bfloat16)
    m_ref[...] += jnp.dot(vbi, tile, preferred_element_type=jnp.float32)

    @pl.when((k == pl.num_programs(0) - 1) & (i == pl.num_programs(1) - 1))
    def _():
        acc = p_ref[...]
        for j in range(m_ref.shape[1] // 128):
            acc = acc + d_ref[:, j * 128:(j + 1) * 128] * m_ref[:, j * 128:(j + 1) * 128]
        p_ref[...] = acc


def block_products(flags, d, di, blocks, tile=1024):
    nb, _, order, _ = blocks.shape
    vecs = d.shape[0]
    grid_spec = pltpu.PrefetchScalarGridSpec(
        num_scalar_prefetch=1,
        grid=(nb, order // tile),
        in_specs=[
            pl.BlockSpec((vecs, order), lambda k, i, f: (0, 0)),
            pl.BlockSpec((None, vecs, tile), lambda k, i, f: (k, 0, i)),
            pl.BlockSpec((None, None, tile, order), lambda k, i, f: (k, 0, i, 0)),
        ],
        out_specs=[
            pl.BlockSpec((None, vecs, tile), lambda k, i, f: (k, 0, i)),
            pl.BlockSpec((vecs, order), lambda k, i, f: (0, 0)),
            pl.BlockSpec((vecs, 128), lambda k, i, f: (0, 0)),
        ],
    )
    return pl.pallas_call(
        products_kernel,
        grid_spec=grid_spec,
        out_shape=[
            jax.ShapeDtypeStruct((nb, vecs, order), jnp.float32),
            jax.ShapeDtypeStruct((vecs, order), jnp.float32),
            jax.ShapeDtypeStruct((vecs, 128), jnp.float32),
        ],
        compiler_params=pltpu.CompilerParams(dimension_semantics=("arbitrary", "arbitrary")),
    )(flags, d, di, blocks)


def pack(blocks, scalars):
    width = blocks[0].shape[1]
    tail = jnp.zeros((PAD, width), jnp.float32).at[0, : scalars.shape[0]].set(scalars)
    return jnp.concatenate(list(blocks) + [tail], axis=0)


def make_on_device(n_row, n_col):
    def on_device(rhs, noise_var, block_rows, kernel_blocks):
        blocks = kernel_blocks[0, 0]
        assert blocks.shape[1] == 1
        rows = block_rows[0]
        nb = rows.shape[0]
        vecs, width = rhs.shape
        col = lax.axis_index("col")
        first_row = lax.axis_index("row") == 0
        flags = (col >= rows).astype(jnp.int32)
        owner = [col == rows[k] for k in range(nb)]
        noise = noise_var[None, :]

        def fetch(res):
            w = width // n_col
            norms = jnp.sum(res * res, axis=1)
            tail = jnp.zeros((PAD, n_col, w), jnp.float32).at[0, :, :vecs].set(jnp.broadcast_to(norms, (n_col, vecs)))
            x = jnp.concatenate([res, tail.reshape(PAD, width)], axis=0)
            y = lax.all_to_all(x, "col", 1, 1, tiled=True)
            norm = jnp.sum(y[vecs].reshape(n_col, w)[:, :vecs], axis=0)
            kept = jnp.concatenate(
                [lax.dynamic_slice_in_dim(y[:vecs], rows[k] * w, w, axis=1) for k in range(nb)], axis=0
            )
            z = lax.all_to_all(jnp.tile(kept, (1, n_col)), "col", 1, 1, tiled=True)
            return z.reshape(nb, vecs, width), norm

        solution = jnp.zeros_like(rhs)
        residual = rhs
        direction = rhs
        dir_rows, norm_now = fetch(rhs)
        for step in range(ITERS):
            fwd, mirrored, lanes = block_products(flags, direction, dir_rows, blocks)
            forward = [fwd[k] for k in range(nb)]
            part = jnp.sum(lanes, axis=1)
            part = part + jnp.where(first_row, jnp.sum(direction * (noise * direction), axis=1), 0.0)
            out = all_reduce(pack(forward, part), "col", n_col)
            terms = mirrored
            for k in range(nb):
                terms = terms + jnp.where(owner[k], out[k * vecs:(k + 1) * vecs], 0.0)
            out = all_reduce(pack([terms], out[nb * vecs, :vecs]), "row", n_row)
            image = noise * direction + out[:vecs]
            curvature = out[vecs, :vecs]
            alpha = norm_now / curvature
            solution = solution + alpha[:, None] * direction
            residual = residual - alpha[:, None] * image
            if step + 1 < ITERS:
                res_rows, norm_next = fetch(residual)
                beta = norm_next / norm_now
                direction = residual + beta[:, None] * direction
                dir_rows = res_rows + beta[None, :, None] * dir_rows
                norm_now = norm_next
        return (solution, residual)

    return on_device


def solution(mesh):
    return jax.shard_map(
        make_on_device(mesh.shape["row"], mesh.shape["col"]),
        mesh=mesh,
        in_specs=(
            P(None, "col"),
            P("col"),
            P("row", None),
            P("row", "col", None, None, None, None),
        ),
        out_specs=(P(None, "col"), P(None, "col")),
        check_vma=False,
    )
```

```python
import jax
import jax.numpy as jnp
from jax import lax
from jax.experimental import pallas as pl
from jax.experimental.pallas import tpu as pltpu
from jax.sharding import PartitionSpec as P

ITERS = 8
PAD = 8


def all_reduce(x, axis, n):
    rows, width = x.shape
    w = width // n
    y = lax.all_to_all(x, axis, 1, 1, tiled=True)
    part = jnp.sum(y.reshape(rows, n, w), axis=1)
    return lax.all_to_all(jnp.tile(part, (1, n)), axis, 1, 1, tiled=True)


def products_kernel(flags_ref, d_ref, di_ref, k_ref, fwd_ref, m_ref, p_ref):
    k = pl.program_id(0)
    i = pl.program_id(1)

    @pl.when((k == 0) & (i == 0))
    def _():
        m_ref[...] = jnp.zeros_like(m_ref)
        p_ref[...] = jnp.zeros_like(p_ref)

    used = flags_ref[k] != 0
    tile = k_ref[...]
    f = lax.dot_general(
        d_ref[...].astype(jnp.bfloat16), tile, (((1,), (1,)), ((), ())), preferred_element_type=jnp.float32
    )
    f = jnp.where(used, f, 0.0)
    fwd_ref[...] = f
    di = di_ref[...]
    acc = p_ref[...]
    for j in range(f.shape[1] // 128):
        acc = acc + di[:, j * 128:(j + 1) * 128] * f[:, j * 128:(j + 1) * 128]
    p_ref[...] = acc
    vbi = jnp.where(used, di, 0.0).astype(jnp.bfloat16)
    m_ref[...] += jnp.dot(vbi, tile, preferred_element_type=jnp.float32)

    @pl.when((k == pl.num_programs(0) - 1) & (i == pl.num_programs(1) - 1))
    def _():
        acc = p_ref[...]
        for j in range(m_ref.shape[1] // 128):
            acc = acc + d_ref[:, j * 128:(j + 1) * 128] * m_ref[:, j * 128:(j + 1) * 128]
        p_ref[...] = acc


def block_products(flags, d, di, blocks, tile=1024):
    nb, _, order, _ = blocks.shape
    vecs = d.shape[0]
    grid_spec = pltpu.PrefetchScalarGridSpec(
        num_scalar_prefetch=1,
        grid=(nb, order // tile),
        in_specs=[
            pl.BlockSpec((vecs, order), lambda k, i, f: (0, 0)),
            pl.BlockSpec((None, vecs, tile), lambda k, i, f: (k, 0, i)),
            pl.BlockSpec((None, None, tile, order), lambda k, i, f: (k, 0, i, 0)),
        ],
        out_specs=[
            pl.BlockSpec((None, vecs, tile), lambda k, i, f: (k, 0, i)),
            pl.BlockSpec((vecs, order), lambda k, i, f: (0, 0)),
            pl.BlockSpec((vecs, 128), lambda k, i, f: (0, 0)),
        ],
    )
    return pl.pallas_call(
        products_kernel,
        grid_spec=grid_spec,
        out_shape=[
            jax.ShapeDtypeStruct((nb, vecs, order), jnp.float32),
            jax.ShapeDtypeStruct((vecs, order), jnp.float32),
            jax.ShapeDtypeStruct((vecs, 128), jnp.float32),
        ],
        compiler_params=pltpu.CompilerParams(dimension_semantics=("arbitrary", "arbitrary")),
    )(flags, d, di, blocks)


def pack(blocks, scalars):
    width = blocks[0].shape[1]
    tail = jnp.zeros((PAD, width), jnp.float32).at[0, : scalars.shape[0]].set(scalars)
    return jnp.concatenate(list(blocks) + [tail], axis=0)


def make_on_device(n_row, n_col):
    def on_device(rhs, noise_var, block_rows, kernel_blocks):
        blocks = kernel_blocks[0, 0]
        assert blocks.shape[1] == 1
        rows = block_rows[0]
        nb = rows.shape[0]
        vecs, width = rhs.shape
        col = lax.axis_index("col")
        first_row = lax.axis_index("row") == 0
        flags = (col >= rows).astype(jnp.int32)
        owner = [col == rows[k] for k in range(nb)]
        noise = noise_var[None, :]

        def fetch(res):
            w = width // n_col
            norms = jnp.sum(res * res, axis=1)
            tail = jnp.zeros((PAD, n_col, w), jnp.float32).at[0, :, :vecs].set(jnp.broadcast_to(norms, (n_col, vecs)))
            x = jnp.concatenate([res, tail.reshape(PAD, width)], axis=0)
            y = lax.all_to_all(x, "col", 1, 1, tiled=True)
            norm = jnp.sum(y[vecs].reshape(n_col, w)[:, :vecs], axis=0)
            kept = jnp.concatenate(
                [lax.dynamic_slice_in_dim(y[:vecs], rows[k] * w, w, axis=1) for k in range(nb)], axis=0
            )
            z = lax.all_to_all(jnp.tile(kept, (1, n_col)), "col", 1, 1, tiled=True)
            return z.reshape(nb, vecs, width), norm

        def step(carry, fetch_next):
            solution, residual, direction, dir_rows, norm_now = carry
            fwd, mirrored, lanes = block_products(flags, direction, dir_rows, blocks)
            forward = [fwd[k] for k in range(nb)]
            part = jnp.sum(lanes, axis=1)
            part = part + jnp.where(first_row, jnp.sum(direction * (noise * direction), axis=1), 0.0)
            out = all_reduce(pack(forward, part), "col", n_col)
            terms = mirrored
            for k in range(nb):
                terms = terms + jnp.where(owner[k], out[k * vecs:(k + 1) * vecs], 0.0)
            out = all_reduce(pack([terms], out[nb * vecs, :vecs]), "row", n_row)
            image = noise * direction + out[:vecs]
            curvature = out[vecs, :vecs]
            alpha = norm_now / curvature
            solution = solution + alpha[:, None] * direction
            residual = residual - alpha[:, None] * image
            if fetch_next:
                res_rows, norm_next = fetch(residual)
                beta = norm_next / norm_now
                direction = residual + beta[:, None] * direction
                dir_rows = res_rows + beta[None, :, None] * dir_rows
                norm_now = norm_next
            return solution, residual, direction, dir_rows, norm_now

        dir_rows, norm_now = fetch(rhs)
        carry = (jnp.zeros_like(rhs), rhs, rhs, dir_rows, norm_now)
        carry = lax.fori_loop(0, ITERS - 1, lambda i, c: step(c, True), carry)
        solution, residual = step(carry, False)[:2]
        return (solution, residual)

    return on_device


def solution(mesh):
    return jax.shard_map(
        make_on_device(mesh.shape["row"], mesh.shape["col"]),
        mesh=mesh,
        in_specs=(
            P(None, "col"),
            P("col"),
            P("row", None),
            P("row", "col", None, None, None, None),
        ),
        out_specs=(P(None, "col"), P(None, "col")),
        check_vma=False,
    )
```

```python
import jax
import jax.numpy as jnp
from jax import lax
from jax.experimental import pallas as pl
from jax.experimental.pallas import tpu as pltpu
from jax.sharding import PartitionSpec as P

ITERS = 8
PAD = 8


def all_reduce(x, axis, n):
    rows, width = x.shape
    w = width // n
    y = lax.all_to_all(x, axis, 1, 1, tiled=True)
    part = jnp.sum(y.reshape(rows, n, w), axis=1)
    return lax.all_to_all(jnp.tile(part, (1, n)), axis, 1, 1, tiled=True)


def products_kernel(flags_ref, d_ref, nz_ref, di_ref, k_ref, fwd_ref, m_ref, p_ref):
    k = pl.program_id(0)
    i = pl.program_id(1)

    @pl.when((k == 0) & (i == 0))
    def _():
        m_ref[...] = jnp.zeros_like(m_ref)
        p_ref[...] = jnp.zeros_like(p_ref)

    used = flags_ref[k] != 0
    tile = k_ref[...]
    f = lax.dot_general(
        d_ref[...].astype(jnp.bfloat16), tile, (((1,), (1,)), ((), ())), preferred_element_type=jnp.float32
    )
    f = jnp.where(used, f, 0.0)
    fwd_ref[...] = f
    di = di_ref[...]
    acc = p_ref[...]
    for j in range(f.shape[1] // 128):
        acc = acc + di[:, j * 128:(j + 1) * 128] * f[:, j * 128:(j + 1) * 128]
    p_ref[...] = acc
    vbi = jnp.where(used, di, 0.0).astype(jnp.bfloat16)
    m_ref[...] += jnp.dot(vbi, tile, preferred_element_type=jnp.float32)

    @pl.when((k == pl.num_programs(0) - 1) & (i == pl.num_programs(1) - 1))
    def _():
        acc = p_ref[...]
        scale = jnp.where(flags_ref[k + 1] != 0, 1.0, 0.0)
        for j in range(m_ref.shape[1] // 128):
            dj = d_ref[:, j * 128:(j + 1) * 128]
            acc = acc + dj * m_ref[:, j * 128:(j + 1) * 128] + scale * (dj * (nz_ref[:, j * 128:(j + 1) * 128] * dj))
        p_ref[...] = acc


def block_products(flags, d, nz, di, blocks, tile=1024):
    nb, _, order, _ = blocks.shape
    vecs = d.shape[0]
    grid_spec = pltpu.PrefetchScalarGridSpec(
        num_scalar_prefetch=1,
        grid=(nb, order // tile),
        in_specs=[
            pl.BlockSpec((vecs, order), lambda k, i, f: (0, 0)),
            pl.BlockSpec((1, order), lambda k, i, f: (0, 0)),
            pl.BlockSpec((None, vecs, tile), lambda k, i, f: (k, 0, i)),
            pl.BlockSpec((None, None, tile, order), lambda k, i, f: (k, 0, i, 0)),
        ],
        out_specs=[
            pl.BlockSpec((None, vecs, tile), lambda k, i, f: (k, 0, i)),
            pl.BlockSpec((vecs, order), lambda k, i, f: (0, 0)),
            pl.BlockSpec((vecs, 128), lambda k, i, f: (0, 0)),
        ],
    )
    return pl.pallas_call(
        products_kernel,
        grid_spec=grid_spec,
        out_shape=[
            jax.ShapeDtypeStruct((nb, vecs, order), jnp.float32),
            jax.ShapeDtypeStruct((vecs, order), jnp.float32),
            jax.ShapeDtypeStruct((vecs, 128), jnp.float32),
        ],
        compiler_params=pltpu.CompilerParams(dimension_semantics=("arbitrary", "arbitrary")),
    )(flags, d, nz, di, blocks)


def pack(blocks, scalars):
    width = blocks[0].shape[1]
    tail = jnp.zeros((PAD, width), jnp.float32).at[0, : scalars.shape[0]].set(scalars)
    return jnp.concatenate(list(blocks) + [tail], axis=0)


def make_on_device(n_row, n_col):
    def on_device(rhs, noise_var, block_rows, kernel_blocks):
        blocks = kernel_blocks[0, 0]
        assert blocks.shape[1] == 1
        rows = block_rows[0]
        nb = rows.shape[0]
        vecs, width = rhs.shape
        col = lax.axis_index("col")
        first_row = lax.axis_index("row") == 0
        flags = jnp.concatenate([(col >= rows).astype(jnp.int32), (lax.axis_index("row") == 0).astype(jnp.int32)[None]])
        owner = [col == rows[k] for k in range(nb)]
        noise = noise_var[None, :]

        def fetch(res):
            w = width // n_col
            norms = jnp.sum(res * res, axis=1)
            tail = jnp.zeros((PAD, n_col, w), jnp.float32).at[0, :, :vecs].set(jnp.broadcast_to(norms, (n_col, vecs)))
            x = jnp.concatenate([res, tail.reshape(PAD, width)], axis=0)
            y = lax.all_to_all(x, "col", 1, 1, tiled=True)
            norm = jnp.sum(y[vecs].reshape(n_col, w)[:, :vecs], axis=0)
            kept = jnp.concatenate(
                [lax.dynamic_slice_in_dim(y[:vecs], rows[k] * w, w, axis=1) for k in range(nb)], axis=0
            )
            z = lax.all_to_all(jnp.tile(kept, (1, n_col)), "col", 1, 1, tiled=True)
            return z.reshape(nb, vecs, width), norm

        solution = jnp.zeros_like(rhs)
        residual = rhs
        direction = rhs
        dir_rows, norm_now = fetch(rhs)
        for step in range(ITERS):
            fwd, mirrored, lanes = block_products(flags, direction, noise, dir_rows, blocks)
            forward = [fwd[k] for k in range(nb)]
            part = jnp.sum(lanes, axis=1)
            out = all_reduce(pack(forward, part), "col", n_col)
            terms = mirrored
            for k in range(nb):
                terms = terms + jnp.where(owner[k], out[k * vecs:(k + 1) * vecs], 0.0)
            out = all_reduce(pack([terms], out[nb * vecs, :vecs]), "row", n_row)
            image = noise * direction + out[:vecs]
            curvature = out[vecs, :vecs]
            alpha = norm_now / curvature
            solution = solution + alpha[:, None] * direction
            residual = residual - alpha[:, None] * image
            if step + 1 < ITERS:
                res_rows, norm_next = fetch(residual)
                beta = norm_next / norm_now
                direction = residual + beta[:, None] * direction
                dir_rows = res_rows + beta[None, :, None] * dir_rows
                norm_now = norm_next
        return (solution, residual)

    return on_device


def solution(mesh):
    return jax.shard_map(
        make_on_device(mesh.shape["row"], mesh.shape["col"]),
        mesh=mesh,
        in_specs=(
            P(None, "col"),
            P("col"),
            P("row", None),
            P("row", "col", None, None, None, None),
        ),
        out_specs=(P(None, "col"), P(None, "col")),
        check_vma=False,
    )
```

```python
import jax
import jax.numpy as jnp
from jax import lax
from jax.experimental import pallas as pl
from jax.experimental.pallas import tpu as pltpu
from jax.sharding import PartitionSpec as P

ITERS = 8
PAD = 8


def all_reduce(x, axis, n):
    rows, width = x.shape
    w = width // n
    y = lax.all_to_all(x, axis, 1, 1, tiled=True)
    part = jnp.sum(y.reshape(rows, n, w), axis=1)
    return lax.all_to_all(jnp.tile(part, (1, n)), axis, 1, 1, tiled=True)


def products_kernel(flags_ref, d_ref, di_ref, k_ref, fwd_ref, m_ref, p_ref):
    k = pl.program_id(0)
    i = pl.program_id(1)

    @pl.when((k == 0) & (i == 0))
    def _():
        m_ref[...] = jnp.zeros_like(m_ref)
        p_ref[...] = jnp.zeros_like(p_ref)

    used = flags_ref[k] != 0
    tile = k_ref[...]
    f = lax.dot_general(
        d_ref[...].astype(jnp.bfloat16), tile, (((1,), (1,)), ((), ())), preferred_element_type=jnp.float32
    )
    f = jnp.where(used, f, 0.0)
    fwd_ref[...] = f
    di = di_ref[...]
    acc = p_ref[...]
    for j in range(f.shape[1] // 128):
        acc = acc + di[:, j * 128:(j + 1) * 128] * f[:, j * 128:(j + 1) * 128]
    p_ref[...] = acc
    vbi = jnp.where(used, di, 0.0).astype(jnp.bfloat16)
    m_ref[...] += jnp.dot(vbi, tile, preferred_element_type=jnp.float32)

    @pl.when((k == pl.num_programs(0) - 1) & (i == pl.num_programs(1) - 1))
    def _():
        acc = p_ref[...]
        for j in range(m_ref.shape[1] // 128):
            acc = acc + d_ref[:, j * 128:(j + 1) * 128] * m_ref[:, j * 128:(j + 1) * 128]
        p_ref[...] = acc


def block_products(flags, d, di, blocks, tile=2048):
    nb, _, order, _ = blocks.shape
    vecs = d.shape[0]
    grid_spec = pltpu.PrefetchScalarGridSpec(
        num_scalar_prefetch=1,
        grid=(nb, order // tile),
        in_specs=[
            pl.BlockSpec((vecs, order), lambda k, i, f: (0, 0)),
            pl.BlockSpec((None, vecs, tile), lambda k, i, f: (k, 0, i)),
            pl.BlockSpec((None, None, tile, order), lambda k, i, f: (k, 0, i, 0)),
        ],
        out_specs=[
            pl.BlockSpec((None, vecs, tile), lambda k, i, f: (k, 0, i)),
            pl.BlockSpec((vecs, order), lambda k, i, f: (0, 0)),
            pl.BlockSpec((vecs, 128), lambda k, i, f: (0, 0)),
        ],
    )
    return pl.pallas_call(
        products_kernel,
        grid_spec=grid_spec,
        out_shape=[
            jax.ShapeDtypeStruct((nb, vecs, order), jnp.float32),
            jax.ShapeDtypeStruct((vecs, order), jnp.float32),
            jax.ShapeDtypeStruct((vecs, 128), jnp.float32),
        ],
        compiler_params=pltpu.CompilerParams(dimension_semantics=("arbitrary", "arbitrary")),
    )(flags, d, di, blocks)


def pack(blocks, scalars):
    width = blocks[0].shape[1]
    tail = jnp.zeros((PAD, width), jnp.float32).at[0, : scalars.shape[0]].set(scalars)
    return jnp.concatenate(list(blocks) + [tail], axis=0)


def make_on_device(n_row, n_col):
    def on_device(rhs, noise_var, block_rows, kernel_blocks):
        blocks = kernel_blocks[0, 0]
        assert blocks.shape[1] == 1
        rows = block_rows[0]
        nb = rows.shape[0]
        vecs, width = rhs.shape
        col = lax.axis_index("col")
        first_row = lax.axis_index("row") == 0
        flags = (col >= rows).astype(jnp.int32)
        owner = [col == rows[k] for k in range(nb)]
        noise = noise_var[None, :]

        def fetch(res):
            w = width // n_col
            norms = jnp.sum(res * res, axis=1)
            tail = jnp.zeros((PAD, n_col, w), jnp.float32).at[0, :, :vecs].set(jnp.broadcast_to(norms, (n_col, vecs)))
            x = jnp.concatenate([res, tail.reshape(PAD, width)], axis=0)
            y = lax.all_to_all(x, "col", 1, 1, tiled=True)
            norm = jnp.sum(y[vecs].reshape(n_col, w)[:, :vecs], axis=0)
            kept = jnp.concatenate(
                [lax.dynamic_slice_in_dim(y[:vecs], rows[k] * w, w, axis=1) for k in range(nb)], axis=0
            )
            z = lax.all_to_all(jnp.tile(kept, (1, n_col)), "col", 1, 1, tiled=True)
            return z.reshape(nb, vecs, width), norm

        solution = jnp.zeros_like(rhs)
        residual = rhs
        direction = rhs
        dir_rows, norm_now = fetch(rhs)
        for step in range(ITERS):
            fwd, mirrored, lanes = block_products(flags, direction, dir_rows, blocks)
            forward = [fwd[k] for k in range(nb)]
            part = jnp.sum(lanes, axis=1)
            part = part + jnp.where(first_row, jnp.sum(direction * (noise * direction), axis=1), 0.0)
            out = all_reduce(pack(forward, part), "col", n_col)
            terms = mirrored
            for k in range(nb):
                terms = terms + jnp.where(owner[k], out[k * vecs:(k + 1) * vecs], 0.0)
            out = all_reduce(pack([terms], out[nb * vecs, :vecs]), "row", n_row)
            image = noise * direction + out[:vecs]
            curvature = out[vecs, :vecs]
            alpha = norm_now / curvature
            solution = solution + alpha[:, None] * direction
            residual = residual - alpha[:, None] * image
            if step + 1 < ITERS:
                res_rows, norm_next = fetch(residual)
                beta = norm_next / norm_now
                direction = residual + beta[:, None] * direction
                dir_rows = res_rows + beta[None, :, None] * dir_rows
                norm_now = norm_next
        return (solution, residual)

    return on_device


def solution(mesh):
    return jax.shard_map(
        make_on_device(mesh.shape["row"], mesh.shape["col"]),
        mesh=mesh,
        in_specs=(
            P(None, "col"),
            P("col"),
            P("row", None),
            P("row", "col", None, None, None, None),
        ),
        out_specs=(P(None, "col"), P(None, "col")),
        check_vma=False,
    )
```
